128 devices in a mesh: dp: 2 (over x_hi), pipe: 4 (over z), tensor: 16 (over y, x_lo, core).
Axes of the slice: x: 4 (x_hi: 2, x_lo: 2; x = x_hi * 2 + x_lo), y: 4, z: 4, core: 2. Of those that a mesh axis runs over, the one named last changes fastest.
Arguments:
- tokens: bfloat16 [2, 4, 2048, 4096], P('dp', 'pipe', 'tensor'), may hold values from -6 to 6
- norm_gain: float32 [4, 4096], P('pipe'), may hold values from 0.25 to 1.75
- query_weight: bfloat16 [4, 4096, 6144], P('pipe', None, 'tensor'), may hold values from -5.625 to 5.625
- kv_weight: bfloat16 [4, 4096, 2048], P('pipe'), may hold values from -0.09375 to 0.09375
- out_weight: bfloat16 [4, 6144, 4096], P('pipe', 'tensor'), may hold values from -0.75 to 0.75
Outputs:
- next_input: bfloat16 [2, 4, 2048, 4096], P('dp', 'pipe', 'tensor')
- max_logits: float32 [4, 48], P('pipe', 'tensor')
The draws below stay inside these ranges and needn't reach their ends.
All inputs are finite; a program needn't handle non-finite values.
Results may differ from the reference program's by a relative error of at most 0.018.
The reference program's roundings to bfloat16 on the way count: a program that leaves them out, or rounds other values in their place, can miss the bound.
Values may be sent and summed in bfloat16 or wider, within the bound.
No kernel may reach another device: no remote copies, remote signals or barrier semaphores. Data moves between devices by JAX's collectives and lax.ppermute only.
A program may use at most 128 MiB of HBM per device.

```python
import math
import jax
import jax.numpy as jnp
from jax import lax

D = 4096
HEADS = 48
KV_HEADS = 8
HD = 128
SEQ = 2048
GROUP = 6
N_DP = 2
N_PIPE = 4
N_TENSOR = 16


def draw_query_weight(key, part):
    base_key = jax.random.fold_in(key, 11)
    values = jnp.clip(jax.random.normal(base_key, (N_PIPE, D, HEADS * HD), jnp.float32), -6.0, 6.0) * D ** (-0.5)
    return values.astype(jnp.bfloat16)


def block_scale(key, extent, shards, least, high):
    def one(dim, parts):
        heights = jax.random.uniform(jax.random.fold_in(jax.random.fold_in(key, 6), dim), (parts,), jnp.float32, least / len(shards), high / len(shards))
        return jnp.repeat(jnp.exp(heights), extent[dim] // parts).reshape((-1,) + (1,) * (len(extent) - dim - 1))

    level = one(*shards[0])
    for cut in shards[1:]:
        level = level * one(*cut)
    return level


def noise(own_key, shape, deviation, bound, shards=(), held_as=jnp.bfloat16):
    drawn = jax.random.normal(own_key, shape, jnp.float32) * deviation
    if len(shards) > 0:
        drawn = block_scale(own_key, shape, shards, -0.22, 0.18) * drawn
    return jnp.clip(drawn, min=-bound, max=bound).astype(held_as)


def setup_inputs(seed: int = 0) -> dict:
    streams_of = jax.random.split(jax.random.key(seed), 6)
    return {
        "tokens": noise(streams_of[0], (N_DP, N_PIPE, SEQ, D), 1.0, 6.0, ((0, 2), (1, 4), (2, 16))),
        "norm_gain": jnp.clip(1.0 + 0.15 * jax.random.normal(streams_of[1], (N_PIPE, D), jnp.float32), 0.25, 1.75),
        "query_weight": draw_query_weight(jax.random.fold_in(streams_of[5], 71), 0),
        "kv_weight": noise(streams_of[3], (N_PIPE, D, KV_HEADS * 2 * HD), D ** -0.5, 0.09375, ((0, 4),)),
        "out_weight": noise(streams_of[4], (N_PIPE, HEADS * HD, D), (HD // 2) ** -0.5, 0.75, ((0, 4), (1, 16))),
    }


def section_block(inputs, gain_row, query_mat, kv_mat, out_mat):
    seq_len = inputs.shape[0]
    wide_in = inputs.astype(jnp.float32)
    normed = (wide_in * lax.rsqrt(lax.optimization_barrier(jnp.mean(wide_in * wide_in, axis=1, keepdims=True)) + 1e-05) * gain_row[None, :].astype(jnp.float32)).astype(jnp.bfloat16)
    queries = jnp.dot(normed, query_mat, preferred_element_type=jnp.float32).astype(jnp.bfloat16)
    keyvals = jnp.dot(normed, kv_mat, preferred_element_type=jnp.float32).astype(jnp.bfloat16)
    query_heads = queries.reshape(seq_len, KV_HEADS, GROUP, HD).astype(jnp.float32)
    kv_heads = keyvals.reshape(seq_len, KV_HEADS, 2, HD).astype(jnp.float32)
    key_heads = kv_heads[:, :, 0]
    value_heads = kv_heads[:, :, 1]
    block_rows = min(512, seq_len)
    score_scale = 1.0 / math.sqrt(HD)

    def attend(row_start):
        query_block = lax.dynamic_slice_in_dim(query_heads, row_start, block_rows, 0)
        scores = jnp.einsum('qkgd,skd->kgqs', query_block, key_heads) * score_scale
        row_ids = row_start + jnp.arange(block_rows)
        col_ids = jnp.arange(seq_len)
        allowed = col_ids[None, :] <= row_ids[:, None]
        scores = jnp.where(allowed, scores, -jnp.inf)
        row_max = lax.optimization_barrier(jnp.max(scores, axis=3, keepdims=True))
        expw = jnp.exp(scores - row_max)
        row_sum = lax.optimization_barrier(jnp.sum(expw, axis=3, keepdims=True))
        rounded = lax.optimization_barrier(expw.astype(jnp.bfloat16)).astype(jnp.float32)
        blended = jnp.einsum('kgqs,skd->qkgd', rounded, value_heads)
        blended = blended / jnp.transpose(row_sum, (2, 0, 1, 3))
        return (blended.astype(jnp.bfloat16), lax.optimization_barrier(jnp.max(row_max[..., 0], axis=2)))
    starts = jnp.arange(seq_len // block_rows) * block_rows
    outputs, head_peaks = lax.map(attend, starts)
    attended = outputs.reshape(seq_len, HEADS * HD)
    peaks_all = lax.optimization_barrier(jnp.max(head_peaks, axis=0)).reshape(HEADS)
    group_cols = HEADS * HD // N_TENSOR
    head_parts = jnp.transpose(attended.reshape(seq_len, N_TENSOR, group_cols), (1, 0, 2))
    weight_parts = out_mat.reshape(N_TENSOR, group_cols, out_mat.shape[1])

    def accumulate(running, operands):
        part_rows, part_weight = operands
        partial_value = jnp.dot(part_rows, part_weight, preferred_element_type=jnp.float32)
        partial_value = lax.optimization_barrier(partial_value.astype(jnp.bfloat16)).astype(jnp.float32)
        return (running + partial_value, None)
    summed, _ = lax.scan(accumulate, jnp.zeros((seq_len, out_mat.shape[1]), jnp.float32), (head_parts, weight_parts))
    return ((wide_in + summed).astype(jnp.bfloat16), peaks_all)

def reference(tokens, norm_gain, query_weight, kv_weight, out_weight):
    results = []
    peak_rows = []
    for group_id in range(N_DP):
        section_outs = []
        section_peaks = []
        for section_id in range(N_PIPE):
            section_out, section_peak = section_block(tokens[group_id, section_id], norm_gain[section_id], query_weight[section_id], kv_weight[section_id], out_weight[section_id])
            section_outs.append(section_out)
            section_peaks.append(section_peak)
        results.append(jnp.stack(section_outs, 0))
        peak_rows.append(jnp.stack(section_peaks, 0))
    block_out = jnp.stack(results, 0)
    next_input = jnp.roll(block_out, 1, axis=1)
    max_logits = lax.optimization_barrier(jnp.max(jnp.stack(peak_rows, 0), axis=0))
    return (next_input, max_logits)
```

```python
import math

import jax
import jax.numpy as jnp
from jax import lax
from jax.sharding import PartitionSpec as P

HD = 128
GROUP = 6
N_BLOCKS = 4


def from_behind(block, axis, distance):
    devices = range(lax.axis_size(axis))
    route = [((i - distance) % len(devices), i) for i in devices]
    return lax.ppermute(block, axis, route)


def on_device(tokens, norm_gain, query_weight, kv_weight, out_weight):
    inputs = tokens[0, 0]
    wide_in = inputs.astype(jnp.float32)
    normed = (
        wide_in
        * lax.rsqrt(jnp.mean(wide_in * wide_in, axis=1, keepdims=True) + 1e-05)
        * norm_gain[0][None, :]
    ).astype(jnp.bfloat16)
    query_local = query_weight[0]
    heads_dev = query_local.shape[1] // HD
    kv_dev = max(1, heads_dev // GROUP)
    kv_cols = kv_dev * 2 * HD
    query_cols = heads_dev * HD
    n_tensor = lax.axis_size("tensor")
    tensor_id = lax.axis_index("tensor")
    kv_start = tensor_id * heads_dev // GROUP
    kv_local = lax.dynamic_slice_in_dim(kv_weight[0], kv_start * 2 * HD, kv_cols, 1)
    joined = jnp.concatenate([query_local, kv_local], 1)
    projected = jnp.dot(
        lax.all_gather(normed, "tensor", axis=0, tiled=True),
        joined,
        preferred_element_type=jnp.float32,
    ).astype(jnp.bfloat16)
    queries = projected[:, :query_cols]
    keyvals = projected[:, query_cols:]
    seq_len = queries.shape[0]
    local_rows = inputs.shape[0]
    group_loc = heads_dev // kv_dev
    query_heads = queries.reshape(seq_len, kv_dev, group_loc, HD)
    kv_heads = keyvals.reshape(seq_len, kv_dev, 2, HD)
    key_heads = kv_heads[:, :, 0]
    value_heads = kv_heads[:, :, 1]
    score_scale = 1.0 / math.sqrt(HD)
    out_local = out_weight[0]
    sub = local_rows // N_BLOCKS
    block_rows = n_tensor * sub
    col_ids = jnp.arange(seq_len)
    pieces = []
    peaks = []
    for b in range(N_BLOCKS):
        query_block = query_heads.reshape(n_tensor, local_rows, kv_dev, group_loc, HD)[
            :, b * sub : (b + 1) * sub
        ].reshape(block_rows, kv_dev, group_loc, HD)
        row_ids = (
            jnp.arange(n_tensor)[:, None] * local_rows + b * sub + jnp.arange(sub)[None, :]
        ).reshape(block_rows)
        scores = (
            jnp.einsum("qkgd,skd->kgqs", query_block, key_heads, preferred_element_type=jnp.float32)
            * score_scale
        )
        allowed = col_ids[None, :] <= row_ids[:, None]
        scores = jnp.where(allowed, scores, -jnp.inf)
        row_max = jnp.max(scores, axis=3, keepdims=True)
        expw = jnp.exp(scores - row_max)
        row_sum = jnp.sum(expw, axis=3, keepdims=True)
        blended = jnp.einsum(
            "kgqs,skd->qkgd",
            expw.astype(jnp.bfloat16),
            value_heads,
            preferred_element_type=jnp.float32,
        )
        blended = blended / jnp.transpose(row_sum, (2, 0, 1, 3))
        attended = blended.astype(jnp.bfloat16).reshape(block_rows, query_cols)
        peaks.append(jnp.max(row_max[..., 0], axis=2))
        partial = jnp.dot(attended, out_local, preferred_element_type=jnp.float32).astype(jnp.bfloat16)
        summed = lax.psum_scatter(partial, "tensor", scatter_dimension=0, tiled=True).astype(jnp.float32)
        result = (wide_in[b * sub : (b + 1) * sub] + summed).astype(jnp.bfloat16)
        pieces.append(from_behind(result, "pipe", 1))
    peaks_local = jnp.max(jnp.stack(peaks), axis=0)
    peak_all = jnp.maximum(peaks_local, from_behind(peaks_local, "dp", 1))
    passed = jnp.concatenate(pieces, 0)
    return (passed[None, None], peak_all)


def solution(mesh):
    placed = (
        P("dp", "pipe", "tensor", None),
        P("pipe", None),
        P("pipe", None, "tensor"),
        P("pipe", None, None),
        P("pipe", "tensor", None),
    )
    return jax.shard_map(
        on_device,
        mesh=mesh,
        in_specs=placed,
        out_specs=(P("dp", "pipe", "tensor", None), P("pipe", "tensor")),
        check_vma=False,
    )
```

```python
import math

import jax
import jax.numpy as jnp
from jax import lax
from jax.sharding import Mesh
from jax.sharding import PartitionSpec as P

HD = 128
GROUP = 6
CHIPS = ("ty", "tx")
CORE = "tc"
TENSOR = CHIPS + (CORE,)


def from_behind(block, axis, distance):
    devices = range(lax.axis_size(axis))
    route = [((i - distance) % len(devices), i) for i in devices]
    return lax.ppermute(block, axis, route)


def scatter_sum(partial):
    n_chips = lax.axis_size(CHIPS)
    rows = partial.shape[0] // (2 * n_chips)
    core = lax.axis_index(CORE)
    halves = partial.reshape(n_chips, 2, rows, partial.shape[1])
    keep = lax.dynamic_index_in_dim(halves, core, 1, keepdims=False)
    give = lax.dynamic_index_in_dim(halves, 1 - core, 1, keepdims=False)
    got = lax.ppermute(give, CORE, [(0, 1), (1, 0)])
    pair = (keep.astype(jnp.float32) + got.astype(jnp.float32)).astype(jnp.bfloat16)
    swapped = lax.all_to_all(pair, CHIPS, 0, 0, tiled=True)
    return jnp.sum(swapped.astype(jnp.float32), 0)


def on_device(tokens, norm_gain, query_weight, kv_weight, out_weight):
    inputs = tokens[0, 0]
    wide_in = inputs.astype(jnp.float32)
    normed = (
        wide_in
        * lax.rsqrt(jnp.mean(wide_in * wide_in, axis=1, keepdims=True) + 1e-05)
        * norm_gain[0][None, :]
    ).astype(jnp.bfloat16)
    query_local = query_weight[0]
    heads_dev = query_local.shape[1] // HD
    kv_dev = max(1, heads_dev // GROUP)
    kv_cols = kv_dev * 2 * HD
    query_cols = heads_dev * HD
    tensor_id = lax.axis_index(TENSOR)
    kv_start = tensor_id * heads_dev // GROUP
    kv_local = lax.dynamic_slice_in_dim(kv_weight[0], kv_start * 2 * HD, kv_cols, 1)
    joined = jnp.concatenate([query_local, kv_local], 1)
    projected = jnp.dot(
        lax.all_gather(normed, TENSOR, axis=0, tiled=True),
        joined,
        preferred_element_type=jnp.float32,
    ).astype(jnp.bfloat16)
    queries = projected[:, :query_cols]
    keyvals = projected[:, query_cols:]
    seq_len = queries.shape[0]
    group_loc = heads_dev // kv_dev
    query_heads = queries.reshape(seq_len, kv_dev, group_loc, HD)
    kv_heads = keyvals.reshape(seq_len, kv_dev, 2, HD)
    key_heads = kv_heads[:, :, 0]
    value_heads = kv_heads[:, :, 1]
    block_rows = min(512, seq_len)
    score_scale = 1.0 / math.sqrt(HD)

    def attend(row_start):
        query_block = lax.dynamic_slice_in_dim(query_heads, row_start, block_rows, 0)
        scores = (
            jnp.einsum("qkgd,skd->kgqs", query_block, key_heads, preferred_element_type=jnp.float32)
            * score_scale
        )
        row_ids = row_start + jnp.arange(block_rows)
        col_ids = jnp.arange(seq_len)
        allowed = col_ids[None, :] <= row_ids[:, None]
        scores = jnp.where(allowed, scores, -jnp.inf)
        row_max = jnp.max(scores, axis=3, keepdims=True)
        expw = jnp.exp(scores - row_max)
        row_sum = jnp.sum(expw, axis=3, keepdims=True)
        blended = jnp.einsum(
            "kgqs,skd->qkgd",
            expw.astype(jnp.bfloat16),
            value_heads,
            preferred_element_type=jnp.float32,
        )
        blended = blended / jnp.transpose(row_sum, (2, 0, 1, 3))
        return (blended.astype(jnp.bfloat16), jnp.max(row_max[..., 0], axis=2))

    starts = jnp.arange(seq_len // block_rows) * block_rows
    outputs, head_peaks = lax.map(attend, starts)
    attended = outputs.reshape(seq_len, query_cols)
    peaks_local = jnp.max(head_peaks, axis=0)
    peak_all = jnp.maximum(peaks_local, from_behind(peaks_local, "dp", 1))
    out_local = out_weight[0]
    summed = scatter_sum(
        jnp.dot(attended, out_local, preferred_element_type=jnp.float32).astype(jnp.bfloat16)
    )
    result = (wide_in + summed).astype(jnp.bfloat16)
    passed = from_behind(result, "pipe", 1)
    return (passed[None, None], peak_all)


def solution(mesh):
    n_tensor = mesh.shape["tensor"]
    fine = Mesh(
        mesh.devices.reshape(mesh.shape["dp"], mesh.shape["pipe"], n_tensor // 4, 2, 2),
        ("dp", "pipe") + TENSOR,
    )
    placed = (
        P("dp", "pipe", TENSOR, None),
        P("pipe", None),
        P("pipe", None, TENSOR),
        P("pipe", None, None),
        P("pipe", TENSOR, None),
    )
    return jax.shard_map(
        on_device,
        mesh=fine,
        in_specs=placed,
        out_specs=(P("dp", "pipe", TENSOR, None), P("pipe", TENSOR)),
        check_vma=False,
    )
```

```python
import math

import jax
import jax.numpy as jnp
from jax import lax
from jax.sharding import Mesh
from jax.sharding import PartitionSpec as P


HD = 128
GROUP = 6
CHIPS = ("ty", "tx")
CORE = "tc"
TENSOR = CHIPS + (CORE,)
N_BLOCKS = 2


def from_behind(block, axis, distance):
    devices = range(lax.axis_size(axis))
    route = [((i - distance) % len(devices), i) for i in devices]
    return lax.ppermute(block, axis, route)


def scatter_sum(partial):
    n_chips = lax.axis_size(CHIPS)
    rows = partial.shape[0] // (2 * n_chips)
    core = lax.axis_index(CORE)
    halves = partial.reshape(n_chips, 2, rows, partial.shape[1])
    keep = lax.dynamic_index_in_dim(halves, core, 1, keepdims=False)
    give = lax.dynamic_index_in_dim(halves, 1 - core, 1, keepdims=False)
    got = lax.ppermute(give, CORE, [(0, 1), (1, 0)])
    pair = (keep.astype(jnp.float32) + got.astype(jnp.float32)).astype(jnp.bfloat16)
    chip = lax.axis_index(CHIPS)
    total = lax.dynamic_index_in_dim(pair, chip, 0, keepdims=False).astype(jnp.float32)
    for k in range(1, n_chips):
        send = lax.dynamic_index_in_dim(pair, (chip + k) % n_chips, 0, keepdims=False)
        route = [(i, (i + k) % n_chips) for i in range(n_chips)]
        got = lax.ppermute(send, CHIPS, route)
        total = total + got.astype(jnp.float32)
    return total


def on_device_body(tokens, norm_gain, query_weight, kv_weight, out_weight):
    inputs = tokens[0, 0]
    wide_in = inputs.astype(jnp.float32)
    normed = (
        wide_in
        * lax.rsqrt(jnp.mean(wide_in * wide_in, axis=1, keepdims=True) + 1e-05)
        * norm_gain[0][None, :]
    ).astype(jnp.bfloat16)
    query_local = query_weight[0]
    heads_dev = query_local.shape[1] // HD
    kv_dev = max(1, heads_dev // GROUP)
    kv_cols = kv_dev * 2 * HD
    query_cols = heads_dev * HD
    tensor_id = lax.axis_index(TENSOR)
    kv_start = tensor_id * heads_dev // GROUP
    kv_local = lax.dynamic_slice_in_dim(kv_weight[0], kv_start * 2 * HD, kv_cols, 1)
    joined = jnp.concatenate([query_local, kv_local], 1)
    projected = jnp.dot(
        lax.all_gather(normed, TENSOR, axis=0, tiled=True),
        joined,
        preferred_element_type=jnp.float32,
    ).astype(jnp.bfloat16)
    queries = projected[:, :query_cols]
    keyvals = projected[:, query_cols:]
    seq_len = queries.shape[0]
    group_loc = heads_dev // kv_dev
    query_heads = queries.reshape(seq_len, kv_dev, group_loc, HD)
    kv_heads = keyvals.reshape(seq_len, kv_dev, 2, HD)
    key_heads = kv_heads[:, :, 0]
    value_heads = kv_heads[:, :, 1]
    score_scale = 1.0 / math.sqrt(HD)
    out_local = out_weight[0]
    n_dev = lax.axis_size(TENSOR)
    local_rows = inputs.shape[0]
    sub = local_rows // N_BLOCKS
    block_rows = n_dev * sub
    col_ids = jnp.arange(seq_len)
    pieces = []
    peaks = []
    for b in range(N_BLOCKS):
        query_block = query_heads.reshape(n_dev, local_rows, kv_dev, group_loc, HD)[
            :, b * sub : (b + 1) * sub
        ].reshape(block_rows, kv_dev, group_loc, HD)
        row_ids = (
            jnp.arange(n_dev)[:, None] * local_rows + b * sub + jnp.arange(sub)[None, :]
        ).reshape(block_rows)
        scores = (
            jnp.einsum("qkgd,skd->kgqs", query_block, key_heads, preferred_element_type=jnp.float32)
            * score_scale
        )
        allowed = col_ids[None, :] <= row_ids[:, None]
        scores = jnp.where(allowed, scores, -jnp.inf)
        row_max = jnp.max(scores, axis=3, keepdims=True)
        expw = jnp.exp(scores - row_max)
        row_sum = jnp.sum(expw, axis=3, keepdims=True)
        blended = jnp.einsum(
            "kgqs,skd->qkgd",
            expw.astype(jnp.bfloat16),
            value_heads,
            preferred_element_type=jnp.float32,
        )
        blended = blended / jnp.transpose(row_sum, (2, 0, 1, 3))
        attended = blended.astype(jnp.bfloat16).reshape(block_rows, query_cols)
        peaks.append(jnp.max(row_max[..., 0], axis=2))
        partial = jnp.dot(attended, out_local, preferred_element_type=jnp.float32).astype(jnp.bfloat16)
        summed = scatter_sum(partial)
        result = (wide_in[b * sub : (b + 1) * sub] + summed).astype(jnp.bfloat16)
        pieces.append(from_behind(result, "pipe", 1))
    peaks_local = jnp.max(jnp.stack(peaks), axis=0)
    peak_all = jnp.maximum(peaks_local, from_behind(peaks_local, "dp", 1))
    passed = jnp.concatenate(pieces, 0)
    return (passed[None, None], peak_all)


def solution(mesh):
    n_tensor = mesh.shape["tensor"]
    fine = Mesh(
        mesh.devices.reshape(mesh.shape["dp"], mesh.shape["pipe"], n_tensor // 4, 2, 2),
        ("dp", "pipe") + TENSOR,
    )
    placed = (
        P("dp", "pipe", TENSOR, None),
        P("pipe", None),
        P("pipe", None, TENSOR),
        P("pipe", None, None),
        P("pipe", TENSOR, None),
    )
    return jax.shard_map(
        on_device_body,
        mesh=fine,
        in_specs=placed,
        out_specs=(P("dp", "pipe", TENSOR, None), P("pipe", TENSOR)),
        check_vma=False,
    )
```

```python
import math

import jax
import jax.numpy as jnp
from jax import lax
from jax.sharding import Mesh
from jax.sharding import PartitionSpec as P


HD = 128
GROUP = 6
CHIPS = ("ty", "tx")
CORE = "tc"
TENSOR = CHIPS + (CORE,)
N_BLOCKS = 4


def from_behind(block, axis, distance):
    devices = range(lax.axis_size(axis))
    route = [((i - distance) % len(devices), i) for i in devices]
    return lax.ppermute(block, axis, route)


def scatter_sum(partial):
    n_y = lax.axis_size("ty")
    rows = partial.shape[0] // (4 * n_y)
    cols = partial.shape[1]
    core = lax.axis_index(CORE)
    halves = partial.reshape(n_y, 2, 2, rows, cols)
    keep = lax.dynamic_index_in_dim(halves, core, 2, keepdims=False)
    give = lax.dynamic_index_in_dim(halves, 1 - core, 2, keepdims=False)
    got = lax.ppermute(give, CORE, [(0, 1), (1, 0)])
    pair = (keep.astype(jnp.float32) + got.astype(jnp.float32)).astype(jnp.bfloat16)
    x_pos = lax.axis_index("tx")
    keep = lax.dynamic_index_in_dim(pair, x_pos, 1, keepdims=False)
    give = lax.dynamic_index_in_dim(pair, 1 - x_pos, 1, keepdims=False)
    got = lax.ppermute(give, "tx", [(0, 1), (1, 0)])
    quad = (keep.astype(jnp.float32) + got.astype(jnp.float32)).astype(jnp.bfloat16)
    y_pos = lax.axis_index("ty")
    total = lax.dynamic_index_in_dim(quad, y_pos, 0, keepdims=False).astype(jnp.float32)
    for k in range(1, n_y):
        send = lax.dynamic_index_in_dim(quad, (y_pos + k) % n_y, 0, keepdims=False)
        route = [(i, (i + k) % n_y) for i in range(n_y)]
        got = lax.ppermute(send, "ty", route)
        total = total + got.astype(jnp.float32)
    return total


def on_device_body(tokens, norm_gain, query_weight, kv_weight, out_weight):
    inputs = tokens[0, 0]
    wide_in = inputs.astype(jnp.float32)
    normed = (
        wide_in
        * lax.rsqrt(jnp.mean(wide_in * wide_in, axis=1, keepdims=True) + 1e-05)
        * norm_gain[0][None, :]
    ).astype(jnp.bfloat16)
    query_local = query_weight[0]
    heads_dev = query_local.shape[1] // HD
    kv_dev = max(1, heads_dev // GROUP)
    kv_cols = kv_dev * 2 * HD
    query_cols = heads_dev * HD
    tensor_id = lax.axis_index(TENSOR)
    kv_start = tensor_id * heads_dev // GROUP
    kv_local = lax.dynamic_slice_in_dim(kv_weight[0], kv_start * 2 * HD, kv_cols, 1)
    joined = jnp.concatenate([query_local, kv_local], 1)
    projected = jnp.dot(
        lax.all_gather(normed, TENSOR, axis=0, tiled=True),
        joined,
        preferred_element_type=jnp.float32,
    ).astype(jnp.bfloat16)
    queries = projected[:, :query_cols]
    keyvals = projected[:, query_cols:]
    seq_len = queries.shape[0]
    group_loc = heads_dev // kv_dev
    query_heads = queries.reshape(seq_len, kv_dev, group_loc, HD)
    kv_heads = keyvals.reshape(seq_len, kv_dev, 2, HD)
    key_heads = kv_heads[:, :, 0]
    value_heads = kv_heads[:, :, 1]
    score_scale = 1.0 / math.sqrt(HD)
    out_local = out_weight[0]
    n_dev = lax.axis_size(TENSOR)
    local_rows = inputs.shape[0]
    sub = local_rows // N_BLOCKS
    block_rows = n_dev * sub
    col_ids = jnp.arange(seq_len)
    pieces = []
    peaks = []
    for b in range(N_BLOCKS):
        query_block = query_heads.reshape(n_dev, local_rows, kv_dev, group_loc, HD)[
            :, b * sub : (b + 1) * sub
        ].reshape(block_rows, kv_dev, group_loc, HD)
        row_ids = (
            jnp.arange(n_dev)[:, None] * local_rows + b * sub + jnp.arange(sub)[None, :]
        ).reshape(block_rows)
        scores = (
            jnp.einsum("qkgd,skd->kgqs", query_block, key_heads, preferred_element_type=jnp.float32)
            * score_scale
        )
        allowed = col_ids[None, :] <= row_ids[:, None]
        scores = jnp.where(allowed, scores, -jnp.inf)
        row_max = jnp.max(scores, axis=3, keepdims=True)
        expw = jnp.exp(scores - row_max)
        row_sum = jnp.sum(expw, axis=3, keepdims=True)
        blended = jnp.einsum(
            "kgqs,skd->qkgd",
            expw.astype(jnp.bfloat16),
            value_heads,
            preferred_element_type=jnp.float32,
        )
        blended = blended / jnp.transpose(row_sum, (2, 0, 1, 3))
        attended = blended.astype(jnp.bfloat16).reshape(block_rows, query_cols)
        peaks.append(jnp.max(row_max[..., 0], axis=2))
        partial = jnp.dot(attended, out_local, preferred_element_type=jnp.float32).astype(jnp.bfloat16)
        summed = scatter_sum(partial)
        result = (wide_in[b * sub : (b + 1) * sub] + summed).astype(jnp.bfloat16)
        pieces.append(from_behind(result, "pipe", 1))
    peaks_local = jnp.max(jnp.stack(peaks), axis=0)
    peak_all = jnp.maximum(peaks_local, from_behind(peaks_local, "dp", 1))
    passed = jnp.concatenate(pieces, 0)
    return (passed[None, None], peak_all)


def solution(mesh):
    n_tensor = mesh.shape["tensor"]
    fine = Mesh(
        mesh.devices.reshape(mesh.shape["dp"], mesh.shape["pipe"], n_tensor // 4, 2, 2),
        ("dp", "pipe") + TENSOR,
    )
    placed = (
        P("dp", "pipe", TENSOR, None),
        P("pipe", None),
        P("pipe", None, TENSOR),
        P("pipe", None, None),
        P("pipe", TENSOR, None),
    )
    return jax.shard_map(
        on_device_body,
        mesh=fine,
        in_specs=placed,
        out_specs=(P("dp", "pipe", TENSOR, None), P("pipe", TENSOR)),
        check_vma=False,
    )
```

```python
import math

import jax
import jax.numpy as jnp
from jax import lax
from jax.sharding import Mesh
from jax.sharding import PartitionSpec as P


HD = 128
GROUP = 6
CHIPS = ("ty", "tx")
CORE = "tc"
TENSOR = CHIPS + (CORE,)
N_BLOCKS = 4
N_QUARTERS = 4


def from_behind(block, axis, distance):
    devices = range(lax.axis_size(axis))
    route = [((i - distance) % len(devices), i) for i in devices]
    return lax.ppermute(block, axis, route)


def scatter_sum(partial):
    n_chips = lax.axis_size(CHIPS)
    rows = partial.shape[0] // (2 * n_chips)
    core = lax.axis_index(CORE)
    halves = partial.reshape(n_chips, 2, rows, partial.shape[1])
    keep = lax.dynamic_index_in_dim(halves, core, 1, keepdims=False)
    give = lax.dynamic_index_in_dim(halves, 1 - core, 1, keepdims=False)
    got = lax.ppermute(give, CORE, [(0, 1), (1, 0)])
    pair = (keep.astype(jnp.float32) + got.astype(jnp.float32)).astype(jnp.bfloat16)
    chip = lax.axis_index(CHIPS)
    total = lax.dynamic_index_in_dim(pair, chip, 0, keepdims=False).astype(jnp.float32)
    for k in range(1, n_chips):
        send = lax.dynamic_index_in_dim(pair, (chip + k) % n_chips, 0, keepdims=False)
        route = [(i, (i + k) % n_chips) for i in range(n_chips)]
        got = lax.ppermute(send, CHIPS, route)
        total = total + got.astype(jnp.float32)
    return total


def on_device_body(tokens, norm_gain, query_weight, kv_weight, out_weight):
    inputs = tokens[0, 0]
    wide_in = inputs.astype(jnp.float32)
    normed = (
        wide_in
        * lax.rsqrt(jnp.mean(wide_in * wide_in, axis=1, keepdims=True) + 1e-05)
        * norm_gain[0][None, :]
    ).astype(jnp.bfloat16)
    query_local = query_weight[0]
    heads_dev = query_local.shape[1] // HD
    kv_dev = max(1, heads_dev // GROUP)
    kv_cols = kv_dev * 2 * HD
    query_cols = heads_dev * HD
    tensor_id = lax.axis_index(TENSOR)
    kv_start = tensor_id * heads_dev // GROUP
    kv_local = lax.dynamic_slice_in_dim(kv_weight[0], kv_start * 2 * HD, kv_cols, 1)
    joined = jnp.concatenate([query_local, kv_local], 1)
    projected = jnp.dot(
        lax.all_gather(normed, TENSOR, axis=0, tiled=True),
        joined,
        preferred_element_type=jnp.float32,
    ).astype(jnp.bfloat16)
    queries = projected[:, :query_cols]
    keyvals = projected[:, query_cols:]
    seq_len = queries.shape[0]
    group_loc = heads_dev // kv_dev
    query_heads = queries.reshape(seq_len, kv_dev, group_loc, HD)
    kv_heads = keyvals.reshape(seq_len, kv_dev, 2, HD)
    key_heads = kv_heads[:, :, 0]
    value_heads = kv_heads[:, :, 1]
    score_scale = 1.0 / math.sqrt(HD)
    out_local = out_weight[0]
    n_dev = lax.axis_size(TENSOR)
    local_rows = inputs.shape[0]
    sub = local_rows // N_BLOCKS
    col_ids = jnp.arange(seq_len)
    pieces = []
    peaks = []
    for b in range(N_BLOCKS):
        rows_of = query_heads.reshape(n_dev, local_rows, kv_dev, group_loc, HD)
        parts = []
        for q in range(N_QUARTERS):
            first = q * n_dev // N_QUARTERS
            last = (q + 1) * n_dev // N_QUARTERS
            key_end = last * local_rows
            query_block = rows_of[first:last, b * sub : (b + 1) * sub].reshape(
                (last - first) * sub, kv_dev, group_loc, HD
            )
            row_ids = (
                jnp.arange(first, last)[:, None] * local_rows
                + b * sub
                + jnp.arange(sub)[None, :]
            ).reshape((last - first) * sub)
            scores = (
                jnp.einsum(
                    "qkgd,skd->kgqs",
                    query_block,
                    key_heads[:key_end],
                    preferred_element_type=jnp.float32,
                )
                * score_scale
            )
            allowed = col_ids[None, :key_end] <= row_ids[:, None]
            scores = jnp.where(allowed, scores, -jnp.inf)
            row_max = jnp.max(scores, axis=3, keepdims=True)
            expw = jnp.exp(scores - row_max)
            row_sum = jnp.sum(expw, axis=3, keepdims=True)
            blended = jnp.einsum(
                "kgqs,skd->qkgd",
                expw.astype(jnp.bfloat16),
                value_heads[:key_end],
                preferred_element_type=jnp.float32,
            )
            blended = blended / jnp.transpose(row_sum, (2, 0, 1, 3))
            parts.append(blended.astype(jnp.bfloat16).reshape(-1, query_cols))
            peaks.append(jnp.max(row_max[..., 0], axis=2))
        attended = jnp.concatenate(parts, 0)
        partial = jnp.dot(attended, out_local, preferred_element_type=jnp.float32).astype(jnp.bfloat16)
        summed = scatter_sum(partial)
        result = (wide_in[b * sub : (b + 1) * sub] + summed).astype(jnp.bfloat16)
        pieces.append(from_behind(result, "pipe", 1))
    peaks_local = jnp.max(jnp.stack(peaks), axis=0)
    peak_all = jnp.maximum(peaks_local, from_behind(peaks_local, "dp", 1))
    passed = jnp.concatenate(pieces, 0)
    return (passed[None, None], peak_all)


def solution(mesh):
    n_tensor = mesh.shape["tensor"]
    fine = Mesh(
        mesh.devices.reshape(mesh.shape["dp"], mesh.shape["pipe"], n_tensor // 4, 2, 2),
        ("dp", "pipe") + TENSOR,
    )
    placed = (
        P("dp", "pipe", TENSOR, None),
        P("pipe", None),
        P("pipe", None, TENSOR),
        P("pipe", None, None),
        P("pipe", TENSOR, None),
    )
    return jax.shard_map(
        on_device_body,
        mesh=fine,
        in_specs=placed,
        out_specs=(P("dp", "pipe", TENSOR, None), P("pipe", TENSOR)),
        check_vma=False,
    )
```

```python
import math

import jax
import jax.numpy as jnp
from jax import lax
from jax.sharding import Mesh
from jax.sharding import PartitionSpec as P


HD = 128
GROUP = 6
CHIPS = ("ty", "tx")
CORE = "tc"
TENSOR = CHIPS + (CORE,)
BLOCK_SPLIT = (56, 48, 24)
N_BLOCKS = len(BLOCK_SPLIT)


def from_behind(block, axis, distance):
    devices = range(lax.axis_size(axis))
    route = [((i - distance) % len(devices), i) for i in devices]
    return lax.ppermute(block, axis, route)


def scatter_sum(partial):
    n_chips = lax.axis_size(CHIPS)
    rows = partial.shape[0] // (2 * n_chips)
    core = lax.axis_index(CORE)
    halves = partial.reshape(n_chips, 2, rows, partial.shape[1])
    keep = lax.dynamic_index_in_dim(halves, core, 1, keepdims=False)
    give = lax.dynamic_index_in_dim(halves, 1 - core, 1, keepdims=False)
    got = lax.ppermute(give, CORE, [(0, 1), (1, 0)])
    pair = (keep.astype(jnp.float32) + got.astype(jnp.float32)).astype(jnp.bfloat16)
    chip = lax.axis_index(CHIPS)
    total = lax.dynamic_index_in_dim(pair, chip, 0, keepdims=False).astype(jnp.float32)
    for k in range(1, n_chips):
        send = lax.dynamic_index_in_dim(pair, (chip + k) % n_chips, 0, keepdims=False)
        route = [(i, (i + k) % n_chips) for i in range(n_chips)]
        got = lax.ppermute(send, CHIPS, route)
        total = total + got.astype(jnp.float32)
    return total


def on_device_body(tokens, norm_gain, query_weight, kv_weight, out_weight):
    inputs = tokens[0, 0]
    wide_in = inputs.astype(jnp.float32)
    normed = (
        wide_in
        * lax.rsqrt(jnp.mean(wide_in * wide_in, axis=1, keepdims=True) + 1e-05)
        * norm_gain[0][None, :]
    ).astype(jnp.bfloat16)
    query_local = query_weight[0]
    heads_dev = query_local.shape[1] // HD
    kv_dev = max(1, heads_dev // GROUP)
    kv_cols = kv_dev * 2 * HD
    query_cols = heads_dev * HD
    tensor_id = lax.axis_index(TENSOR)
    kv_start = tensor_id * heads_dev // GROUP
    kv_local = lax.dynamic_slice_in_dim(kv_weight[0], kv_start * 2 * HD, kv_cols, 1)
    joined = jnp.concatenate([query_local, kv_local], 1)
    projected = jnp.dot(
        lax.all_gather(normed, TENSOR, axis=0, tiled=True),
        joined,
        preferred_element_type=jnp.float32,
    ).astype(jnp.bfloat16)
    queries = projected[:, :query_cols]
    keyvals = projected[:, query_cols:]
    seq_len = queries.shape[0]
    group_loc = heads_dev // kv_dev
    query_heads = queries.reshape(seq_len, kv_dev, group_loc, HD)
    kv_heads = keyvals.reshape(seq_len, kv_dev, 2, HD)
    key_heads = kv_heads[:, :, 0]
    value_heads = kv_heads[:, :, 1]
    score_scale = 1.0 / math.sqrt(HD)
    out_local = out_weight[0]
    n_dev = lax.axis_size(TENSOR)
    local_rows = inputs.shape[0]
    bounds = [0]
    for size in BLOCK_SPLIT:
        bounds.append(bounds[-1] + size * local_rows // sum(BLOCK_SPLIT))
    col_ids = jnp.arange(seq_len)
    pieces = []
    peaks = []
    for b in range(N_BLOCKS):
        lo, hi = bounds[b], bounds[b + 1]
        sub = hi - lo
        block_rows = n_dev * sub
        query_block = query_heads.reshape(n_dev, local_rows, kv_dev, group_loc, HD)[
            :, lo:hi
        ].reshape(block_rows, kv_dev, group_loc, HD)
        row_ids = (
            jnp.arange(n_dev)[:, None] * local_rows + lo + jnp.arange(sub)[None, :]
        ).reshape(block_rows)
        scores = (
            jnp.einsum("qkgd,skd->kgqs", query_block, key_heads, preferred_element_type=jnp.float32)
            * score_scale
        )
        allowed = col_ids[None, :] <= row_ids[:, None]
        scores = jnp.where(allowed, scores, -jnp.inf)
        row_max = jnp.max(scores, axis=3, keepdims=True)
        expw = jnp.exp(scores - row_max)
        row_sum = jnp.sum(expw, axis=3, keepdims=True)
        blended = jnp.einsum(
            "kgqs,skd->qkgd",
            expw.astype(jnp.bfloat16),
            value_heads,
            preferred_element_type=jnp.float32,
        )
        blended = blended / jnp.transpose(row_sum, (2, 0, 1, 3))
        attended = blended.astype(jnp.bfloat16).reshape(block_rows, query_cols)
        peaks.append(jnp.max(row_max[..., 0], axis=2))
        partial = jnp.dot(attended, out_local, preferred_element_type=jnp.float32).astype(jnp.bfloat16)
        summed = scatter_sum(partial)
        result = (wide_in[lo:hi] + summed).astype(jnp.bfloat16)
        pieces.append(from_behind(result, "pipe", 1))
    peaks_local = jnp.max(jnp.stack(peaks), axis=0)
    peak_all = jnp.maximum(peaks_local, from_behind(peaks_local, "dp", 1))
    passed = jnp.concatenate(pieces, 0)
    return (passed[None, None], peak_all)


def solution(mesh):
    n_tensor = mesh.shape["tensor"]
    fine = Mesh(
        mesh.devices.reshape(mesh.shape["dp"], mesh.shape["pipe"], n_tensor // 4, 2, 2),
        ("dp", "pipe") + TENSOR,
    )
    placed = (
        P("dp", "pipe", TENSOR, None),
        P("pipe", None),
        P("pipe", None, TENSOR),
        P("pipe", None, None),
        P("pipe", TENSOR, None),
    )
    return jax.shard_map(
        on_device_body,
        mesh=fine,
        in_specs=placed,
        out_specs=(P("dp", "pipe", TENSOR, None), P("pipe", TENSOR)),
        check_vma=False,
    )
```

```python
import math

import jax
import jax.numpy as jnp
from jax import lax
from jax.sharding import Mesh
from jax.sharding import PartitionSpec as P


HD = 128
CHIPS = ("ty", "tx")
CORE = "tc"
TENSOR = CHIPS + (CORE,)
BLOCK_SPLIT = (56, 48, 24)
N_BLOCKS = len(BLOCK_SPLIT)


def from_behind(block, axis, distance):
    devices = range(lax.axis_size(axis))
    route = [((i - distance) % len(devices), i) for i in devices]
    return lax.ppermute(block, axis, route)


def scatter_sum(partial):
    n_chips = partial.shape[0]
    chip = lax.axis_index(CHIPS)
    total = lax.dynamic_index_in_dim(partial, chip, 0, keepdims=False).astype(jnp.float32)
    for k in range(1, n_chips):
        send = lax.dynamic_index_in_dim(partial, (chip + k) % n_chips, 0, keepdims=False)
        route = [(i, (i + k) % n_chips) for i in range(n_chips)]
        got = lax.ppermute(send, CHIPS, route)
        total = total + got.astype(jnp.float32)
    return total


def other_core(block):
    return lax.ppermute(block, CORE, [(0, 1), (1, 0)])


def on_device_body(tokens, norm_gain, query_weight, kv_weight, out_weight):
    inputs = tokens[0, 0]
    wide_in = inputs.astype(jnp.float32)
    normed = (
        wide_in
        * lax.rsqrt(jnp.mean(wide_in * wide_in, axis=1, keepdims=True) + 1e-05)
        * norm_gain[0][None, :]
    ).astype(jnp.bfloat16)
    query_local = query_weight[0]
    out_local = out_weight[0]
    heads_dev = query_local.shape[1] // HD
    chip_heads = 2 * heads_dev
    query_cols = chip_heads * HD
    chip = lax.axis_index(CHIPS)
    core = lax.axis_index(CORE)
    kv_local = lax.dynamic_slice_in_dim(kv_weight[0], chip * 2 * HD, 2 * HD, 1)
    query_chip = jnp.concatenate([query_local, other_core(query_local)], 1)
    out_chip = jnp.concatenate([out_local, other_core(out_local)], 0)
    gathered = lax.all_gather(normed, TENSOR, axis=0, tiled=True)
    seq_len = gathered.shape[0]
    local_rows = inputs.shape[0]
    n_chips = seq_len // (2 * local_rows)
    own_rows = lax.dynamic_index_in_dim(
        gathered.reshape(n_chips, 2, local_rows, gathered.shape[1]), core, 1, keepdims=False
    )
    projected = jnp.dot(
        own_rows, jnp.concatenate([query_chip, kv_local], 1), preferred_element_type=jnp.float32
    ).astype(jnp.bfloat16)
    queries = projected[..., :query_cols]
    own_kv = projected[..., query_cols:]
    other_kv = other_core(own_kv)
    keyvals = jnp.where(
        core == 0, jnp.stack([own_kv, other_kv], 1), jnp.stack([other_kv, own_kv], 1)
    ).reshape(seq_len, 2 * HD)
    query_heads = queries.reshape(n_chips, local_rows, chip_heads, HD)
    kv_heads = keyvals.reshape(seq_len, 2, HD)
    key_heads = kv_heads[:, 0]
    value_heads = kv_heads[:, 1]
    score_scale = 1.0 / math.sqrt(HD)
    bounds = [0]
    for size in BLOCK_SPLIT:
        bounds.append(bounds[-1] + size * local_rows // sum(BLOCK_SPLIT))
    col_ids = jnp.arange(seq_len)
    pieces = []
    peaks = []
    for b in range(N_BLOCKS):
        lo, hi = bounds[b], bounds[b + 1]
        sub = hi - lo
        block_rows = n_chips * sub
        query_block = query_heads[:, lo:hi].reshape(block_rows, chip_heads, HD)
        row_ids = (
            (jnp.arange(n_chips)[:, None] * 2 + core) * local_rows
            + lo
            + jnp.arange(sub)[None, :]
        ).reshape(block_rows)
        scores = (
            jnp.einsum("qgd,sd->gqs", query_block, key_heads, preferred_element_type=jnp.float32)
            * score_scale
        )
        allowed = col_ids[None, :] <= row_ids[:, None]
        scores = jnp.where(allowed, scores, -jnp.inf)
        row_max = jnp.max(scores, axis=2, keepdims=True)
        expw = jnp.exp(scores - row_max)
        row_sum = jnp.sum(expw, axis=2, keepdims=True)
        blended = jnp.einsum(
            "gqs,sd->qgd",
            expw.astype(jnp.bfloat16),
            value_heads,
            preferred_element_type=jnp.float32,
        )
        blended = blended / jnp.transpose(row_sum, (1, 0, 2))
        attended = blended.astype(jnp.bfloat16).reshape(block_rows, query_cols)
        peaks.append(jnp.max(row_max[..., 0], axis=1))
        partial = jnp.dot(attended, out_chip, preferred_element_type=jnp.float32).astype(jnp.bfloat16)
        summed = scatter_sum(partial.reshape(n_chips, sub, partial.shape[1]))
        result = (wide_in[lo:hi] + summed).astype(jnp.bfloat16)
        pieces.append(from_behind(result, "pipe", 1))
    chip_peaks = jnp.max(jnp.stack(peaks), axis=0)
    own_peaks = jnp.maximum(chip_peaks[:heads_dev], other_core(chip_peaks[heads_dev:]))
    peak_all = jnp.maximum(own_peaks, from_behind(own_peaks, "dp", 1))
    passed = jnp.concatenate(pieces, 0)
    return (passed[None, None], peak_all[None])


def solution(mesh):
    n_tensor = mesh.shape["tensor"]
    fine = Mesh(
        mesh.devices.reshape(mesh.shape["dp"], mesh.shape["pipe"], n_tensor // 4, 2, 2),
        ("dp", "pipe") + TENSOR,
    )
    placed = (
        P("dp", "pipe", TENSOR, None),
        P("pipe", None),
        P("pipe", None, TENSOR),
        P("pipe", None, None),
        P("pipe", TENSOR, None),
    )
    return jax.shard_map(
        on_device_body,
        mesh=fine,
        in_specs=placed,
        out_specs=(P("dp", "pipe", TENSOR, None), P("pipe", TENSOR)),
        check_vma=False,
    )
```

```python
import math

import jax
import jax.numpy as jnp
from jax import lax
from jax.sharding import Mesh
from jax.sharding import PartitionSpec as P


HD = 128
CHIPS = ("ty", "tx")
CORE = "tc"
TENSOR = CHIPS + (CORE,)
BLOCK_SPLIT = (64, 40, 24)
N_BLOCKS = len(BLOCK_SPLIT)


def from_behind(block, axis, distance):
    devices = range(lax.axis_size(axis))
    route = [((i - distance) % len(devices), i) for i in devices]
    return lax.ppermute(block, axis, route)


def scatter_sum(partial):
    n_chips = partial.shape[0]
    chip = lax.axis_index(CHIPS)
    total = lax.dynamic_index_in_dim(partial, chip, 0, keepdims=False).astype(jnp.float32)
    for k in range(1, n_chips):
        send = lax.dynamic_index_in_dim(partial, (chip + k) % n_chips, 0, keepdims=False)
        route = [(i, (i + k) % n_chips) for i in range(n_chips)]
        got = lax.ppermute(send, CHIPS, route)
        total = total + got.astype(jnp.float32)
    return total


def other_core(block):
    return lax.ppermute(block, CORE, [(0, 1), (1, 0)])


def on_device_body(tokens, norm_gain, query_weight, kv_weight, out_weight):
    inputs = tokens[0, 0]
    wide_in = inputs.astype(jnp.float32)
    normed = (
        wide_in
        * lax.rsqrt(jnp.mean(wide_in * wide_in, axis=1, keepdims=True) + 1e-05)
        * norm_gain[0][None, :]
    ).astype(jnp.bfloat16)
    query_local = query_weight[0]
    out_local = out_weight[0]
    heads_dev = query_local.shape[1] // HD
    chip_heads = 2 * heads_dev
    query_cols = chip_heads * HD
    chip = lax.axis_index(CHIPS)
    core = lax.axis_index(CORE)
    kv_local = lax.dynamic_slice_in_dim(kv_weight[0], chip * 2 * HD, 2 * HD, 1)
    query_chip = jnp.concatenate([query_local, other_core(query_local)], 1)
    out_chip = jnp.concatenate([out_local, other_core(out_local)], 0)
    gathered = lax.all_gather(normed, TENSOR, axis=0, tiled=True)
    seq_len = gathered.shape[0]
    local_rows = inputs.shape[0]
    n_chips = seq_len // (2 * local_rows)
    own_rows = lax.dynamic_index_in_dim(
        gathered.reshape(n_chips, 2, local_rows, gathered.shape[1]), core, 1, keepdims=False
    )
    queries = jnp.dot(own_rows, query_chip, preferred_element_type=jnp.float32).astype(jnp.bfloat16)
    keyvals = jnp.dot(gathered, kv_local, preferred_element_type=jnp.float32).astype(jnp.bfloat16)
    query_heads = queries.reshape(n_chips, local_rows, chip_heads, HD)
    kv_heads = keyvals.reshape(seq_len, 2, HD)
    key_heads = kv_heads[:, 0]
    value_heads = kv_heads[:, 1]
    score_scale = 1.0 / math.sqrt(HD)
    bounds = [0]
    for size in BLOCK_SPLIT:
        bounds.append(bounds[-1] + size * local_rows // sum(BLOCK_SPLIT))
    col_ids = jnp.arange(seq_len)
    pieces = []
    peaks = []
    for b in range(N_BLOCKS):
        lo, hi = bounds[b], bounds[b + 1]
        sub = hi - lo
        block_rows = n_chips * sub
        query_block = query_heads[:, lo:hi].reshape(block_rows, chip_heads, HD)
        row_ids = (
            (jnp.arange(n_chips)[:, None] * 2 + core) * local_rows
            + lo
            + jnp.arange(sub)[None, :]
        ).reshape(block_rows)
        scores = (
            jnp.einsum("qgd,sd->gqs", query_block, key_heads, preferred_element_type=jnp.float32)
            * score_scale
        )
        allowed = col_ids[None, :] <= row_ids[:, None]
        scores = jnp.where(allowed, scores, -jnp.inf)
        row_max = jnp.max(scores, axis=2, keepdims=True)
        expw = jnp.exp(scores - row_max)
        row_sum = jnp.sum(expw, axis=2, keepdims=True)
        blended = jnp.einsum(
            "gqs,sd->qgd",
            expw.astype(jnp.bfloat16),
            value_heads,
            preferred_element_type=jnp.float32,
        )
        blended = blended / jnp.transpose(row_sum, (1, 0, 2))
        attended = blended.astype(jnp.bfloat16).reshape(block_rows, query_cols)
        peaks.append(jnp.max(row_max[..., 0], axis=1))
        partial = jnp.dot(attended, out_chip, preferred_element_type=jnp.float32).astype(jnp.bfloat16)
        summed = scatter_sum(partial.reshape(n_chips, sub, partial.shape[1]))
        result = (wide_in[lo:hi] + summed).astype(jnp.bfloat16)
        pieces.append(from_behind(result, "pipe", 1))
    chip_peaks = jnp.max(jnp.stack(peaks), axis=0)
    own_peaks = jnp.maximum(chip_peaks[:heads_dev], other_core(chip_peaks[heads_dev:]))
    peak_all = jnp.maximum(own_peaks, from_behind(own_peaks, "dp", 1))
    passed = jnp.concatenate(pieces, 0)
    return (passed[None, None], peak_all[None])


def solution(mesh):
    n_tensor = mesh.shape["tensor"]
    fine = Mesh(
        mesh.devices.reshape(mesh.shape["dp"], mesh.shape["pipe"], n_tensor // 4, 2, 2),
        ("dp", "pipe") + TENSOR,
    )
    placed = (
        P("dp", "pipe", TENSOR, None),
        P("pipe", None),
        P("pipe", None, TENSOR),
        P("pipe", None, None),
        P("pipe", TENSOR, None),
    )
    return jax.shard_map(
        on_device_body,
        mesh=fine,
        in_specs=placed,
        out_specs=(P("dp", "pipe", TENSOR, None), P("pipe", TENSOR)),
        check_vma=False,
    )
```
